512 devices in a mesh: dp: 64 (over x, z, core), grp: 8 (over y).
Axes of the slice: x: 4, y: 8, z: 8, core: 2. Of those that a mesh axis runs over, the one named last changes fastest.
Arguments:
- tokens: bfloat16 [262144, 1024], P(('dp', 'grp')), may hold values from -24 to 24
- weight: bfloat16 [1024, 512], replicated, may hold values from -0.1875 to 0.1875
- captions: bfloat16 [65536, 512], P(('dp', 'grp')), may hold values from -400 to 400
- block_owner: int32 [64], replicated, may hold values from 0 to 63, each once
- confusable: int32 [64, 14], replicated, may hold values from 0 to 63, as said below
- counts: int32 [64], replicated, may hold values from 1 to 14, as said below
Outputs:
- clip_loss: float32 [65536], P(('dp', 'grp'))
- grad_pooled: float32 [65536, 512], P(('dp', 'grp'))
- grad_w: float32 [1024, 512], P('dp', 'grp')
The draws below stay inside these ranges and needn't reach their ends.
Inputs may be any that keep to these rules, and one draw needn't show every extreme that they name: `block_owner`: a permutation: each dp index holds exactly one caption group. `confusable`: row p holds 14 distinct caption group ids, none equal to p; only the first counts[p] entries are used. `counts`: some clip group uses all 14 entries.
All inputs are finite; a program needn't handle non-finite values.
Results may differ from the reference program's by a relative error of at most 0.035.
The reference program's roundings to bfloat16 on the way count: a program that leaves them out, or rounds other values in their place, can miss the bound.
Values may be sent and summed in bfloat16 or wider, within the bound.
No kernel may reach another device: no remote copies, remote signals or barrier semaphores. Data moves between devices by JAX's collectives and lax.ppermute only.
A program may use at most 64 MiB of HBM per device.

```python
import math
import jax
import jax.numpy as jnp
from jax import lax

D = 1024
E = 512
BR = 128
F = 4
K_MAX = 14
NB = 512
CLIPS = 65536
TOKENS = 262144
N_DP = 64
N_GRP = 8


def draw_captions(key, part):
    row_count = NB * BR
    member_of = jnp.arange(row_count) // BR % N_GRP
    rising = 0.6 * jnp.exp(math.log(3.0) * member_of.astype(jnp.float32) / max(N_GRP - 1, 1))
    values = jnp.clip(jax.random.normal(key, (row_count, E), jnp.float32), -6.0, 6.0)
    return (values * rising[:, None]).astype(jnp.bfloat16)


def permute_one(sub_key):
    return jax.random.permutation(sub_key, N_DP - 1)


def draw_confusable(key, part):
    orders = jax.vmap(permute_one)(jax.random.split(key, N_DP))
    chosen = orders[:, :K_MAX].astype(jnp.int32)
    return ((jnp.arange(N_DP, dtype=jnp.int32)[:, None] + 1 + chosen) % N_DP).astype(jnp.int32)


def draw_counts(key, part):
    drawn = jax.random.randint(key, (N_DP,), 1, K_MAX + 1, dtype=jnp.int32)
    fullest = jax.random.randint(jax.random.fold_in(key, 7), (), 0, N_DP, dtype=jnp.int32)
    return jnp.where(jnp.arange(N_DP, dtype=jnp.int32) == fullest, K_MAX, drawn).astype(jnp.int32)


def spiked(result, key, source, target, shards_of, factor):
    def block_of(position):
        return (jnp.arange(result.shape[position]) // (result.shape[position] // shards_of)).reshape((-1,) + (1,) * (result.ndim - 1 - position))

    first = jax.random.permutation(key, shards_of)[block_of(target)]
    second = (block_of(target) + shards_of // 2) % shards_of
    return jnp.where((block_of(source) == first) | (block_of(source) == second), factor * result, result)


def block_levels(rng, dims, shards, low, high):
    level, own = 1.0, jax.random.fold_in(rng, 6)
    for position, blocks in shards:
        heights = jnp.exp(jax.random.uniform(jax.random.fold_in(own, position), (blocks,), jnp.float32, low / len(shards), high / len(shards)))
        level = level * jnp.repeat(heights, dims[position] // blocks).reshape([-1 if axis == position else 1 for axis in range(len(dims))])
    return level


def gaussian(stream_key, dims, scale, most, cuts=(), kind=jnp.bfloat16):
    level = block_levels(stream_key, dims, cuts, -0.22, 0.18) if cuts else 1.0
    result = jax.random.normal(stream_key, dims, jnp.float32) * scale * level
    return jnp.minimum(jnp.maximum(result, -most), most).astype(kind)


def heavy_noise(stream_key, shape, deviation, limit, pieces, heavy, kind=jnp.bfloat16):
    result = deviation * jax.random.normal(stream_key, shape, jnp.float32)
    if pieces:
        result = result * block_levels(stream_key, shape, pieces, -0.22, 0.18)
    return jnp.clip(spiked(result, jax.random.fold_in(stream_key, 3), *heavy), -limit, limit).astype(kind)


def setup_inputs(seed: int = 0) -> dict:
    key_list = jax.random.split(jax.random.key(seed), 7)
    tokens = heavy_noise(key_list[0], (TOKENS, D), 1.0, 24.0, ((0, 512),), (0, 1, 512, 6.0))
    weight = gaussian(key_list[1], (D, E), D ** -0.5, 0.1875)
    captions = draw_captions(jax.random.fold_in(key_list[6], 71), 0)
    block_owner = jax.random.permutation(key_list[3], N_DP).astype(jnp.int32)
    confusable = draw_confusable(jax.random.fold_in(key_list[6], 71), 0)
    counts = draw_counts(jax.random.fold_in(key_list[6], 71), 0)
    return {"tokens": tokens, "weight": weight, "captions": captions, "block_owner": block_owner, "confusable": confusable, "counts": counts}


SCORE_SCALE = 2.0
EPSILON = 1e-06
FLOOR = -1e+30

def reference(tokens, weight, captions, block_owner, confusable, counts):
    members = N_GRP
    factor = SCORE_SCALE / E ** 0.5
    group_rows = members * BR
    stored = captions.reshape(N_DP, members, BR, E)
    listed = jnp.concatenate([jnp.arange(N_DP, dtype=jnp.int32)[:, None], confusable.astype(jnp.int32)], axis=1)
    slot_count = listed.shape[1] + 1
    diagonal = jnp.eye(members, dtype=jnp.float32)
    highest = lax.Precision.HIGHEST

    def one_group(running, group_index):
        tok_rows = lax.dynamic_slice_in_dim(tokens, group_index * group_rows * F, group_rows * F, 0)
        projected = jnp.dot(tok_rows, weight, preferred_element_type=jnp.float32)
        activated = jax.nn.gelu(projected)
        pooled = lax.optimization_barrier(jnp.mean(activated.reshape(group_rows, F, E), axis=1))
        inverse_rms = lax.rsqrt(lax.optimization_barrier(jnp.mean(pooled * pooled, axis=-1, keepdims=True)) + EPSILON)
        unit_rows = pooled * inverse_rms
        embedded = lax.optimization_barrier(unit_rows.astype(jnp.bfloat16)).astype(jnp.float32)
        sources = block_owner[listed[group_index]].astype(jnp.int32)
        in_group = lax.dynamic_index_in_dim(stored, group_index, 0, keepdims=True)
        caption_slots = jnp.concatenate([in_group, stored[sources]], axis=0)
        caption_slots = jnp.swapaxes(caption_slots, 0, 1).astype(jnp.float32)
        usable = jnp.arange(slot_count) < 2 + counts[group_index]
        scores = factor * jnp.einsum('re,gsce->rgsc', embedded, caption_slots, precision=highest)
        scores = jnp.where(usable[None, None, :, None], scores, FLOOR)
        row_top = lax.optimization_barrier(jnp.max(scores, axis=(1, 2, 3)))
        row_total = lax.optimization_barrier(jnp.sum(jnp.exp(scores - row_top[:, None, None, None]), axis=(1, 2, 3)))
        logsum = row_top + jnp.log(row_total)
        shaped = scores.reshape(members, BR, members, slot_count, BR)
        member_ids = jnp.arange(members)[:, None]
        row_ids = jnp.arange(BR)[None, :]
        positive = shaped[member_ids, row_ids, member_ids, 1, row_ids].reshape(group_rows)
        group_loss = logsum - positive
        weights = jnp.exp(scores - logsum[:, None, None, None])
        weights = lax.optimization_barrier(weights.astype(jnp.bfloat16)).astype(jnp.float32)
        partial_sums = jnp.einsum('rgsc,gsce->rge', weights, caption_slots, precision=highest)
        partial_sums = partial_sums.reshape(members, BR, members, E) - diagonal[:, None, :, None] * caption_slots[:, 1][:, :, None, :]
        rounded = lax.optimization_barrier(partial_sums.astype(jnp.bfloat16)).astype(jnp.float32)
        grad_unit = factor * lax.optimization_barrier(jnp.sum(rounded, axis=2)).reshape(group_rows, E)
        grad_pooled = inverse_rms * (grad_unit - unit_rows * lax.optimization_barrier(jnp.mean(grad_unit * unit_rows, axis=-1, keepdims=True)))
        spread = jnp.broadcast_to(grad_pooled[:, None, :] / F, (group_rows, F, E)).reshape(group_rows * F, E)
        gelu_out, pullback = jax.vjp(jax.nn.gelu, projected)
        grad_projected = pullback(spread)[0].astype(jnp.bfloat16)
        weight_term = lax.dot_general(tok_rows, grad_projected, (((0,), (0,)), ((), ())), preferred_element_type=jnp.float32)
        return (running + weight_term, (group_loss, grad_pooled))
    initial = jnp.zeros((D, E), jnp.float32)
    summed, (losses, gradients) = lax.scan(one_group, initial, jnp.arange(N_DP, dtype=jnp.int32))
    return (losses.reshape(CLIPS), gradients.reshape(CLIPS, E), summed / NB ** 0.5)
```

```python
import jax
import jax.numpy as jnp
from jax import lax
from jax.sharding import PartitionSpec as P

SCORE_SCALE = 2.0
EPSILON = 1e-06
FLOOR = -1e30


def gather_ring(part, axis):
    size = lax.axis_size(axis)
    me = lax.axis_index(axis)
    received = [part]
    for shift in range(1, size):
        pairs = [(i, (i + shift) % size) for i in range(size)]
        received.append(lax.ppermute(part, axis, pairs))
    stacked = jnp.stack(received)
    order = (me - jnp.arange(size, dtype=jnp.int32)) % size
    return jnp.take(stacked, order, axis=0)


def reduce_blocks(blocks, axis):
    swapped = lax.all_to_all(blocks, axis, 0, 0, tiled=True)
    return jnp.sum(swapped.astype(jnp.float32), axis=0)


def on_device(tokens, weight, captions, block_owner, confusable, counts):
    members = lax.axis_size("grp")
    groups = lax.axis_size("dp")
    group_index = lax.axis_index("dp")
    member_index = lax.axis_index("grp")
    block_rows = captions.shape[0]
    width = captions.shape[1]
    depth = tokens.shape[1]
    frames = tokens.shape[0] // block_rows
    factor = SCORE_SCALE / width**0.5
    every_block = lax.all_gather(captions, "dp", axis=0, tiled=False)
    projected = jnp.dot(tokens, weight, preferred_element_type=jnp.float32)
    activated = jax.nn.gelu(projected)
    pooled = jnp.mean(activated.reshape(block_rows, frames, width), axis=1)
    inverse_rms = lax.rsqrt(jnp.mean(pooled * pooled, axis=-1, keepdims=True) + EPSILON)
    unit_rows = pooled * inverse_rms
    embedded = unit_rows.astype(jnp.bfloat16)
    group_clips = gather_ring(embedded, "grp").reshape(members * block_rows, width)
    listed = jnp.concatenate([jnp.arange(groups, dtype=jnp.int32)[:, None], confusable], axis=1)
    slot_count = listed.shape[1] + 1
    sources = block_owner[listed[group_index]]
    fetched = jnp.take(every_block, sources, axis=0)
    caption_slots = jnp.concatenate([captions[None], fetched], axis=0)
    usable = jnp.arange(slot_count, dtype=jnp.int32) < 2 + counts[group_index]
    scores = factor * jnp.einsum(
        "re,sce->rsc", group_clips, caption_slots, preferred_element_type=jnp.float32
    )
    scores = jnp.where(usable[None, :, None], scores, FLOOR)
    row_top = jnp.max(scores, axis=(1, 2))
    row_total = jnp.sum(jnp.exp(scores - row_top[:, None, None]), axis=(1, 2))
    stats = lax.all_gather(jnp.stack([row_top, row_total]), "grp", axis=0, tiled=False)
    row_top = jnp.max(stats[:, 0], axis=0)
    row_total = jnp.sum(stats[:, 1] * jnp.exp(stats[:, 0] - row_top[None]), axis=0)
    logsum = row_top + jnp.log(row_total)
    own_start = member_index * block_rows
    own_scores = lax.dynamic_slice_in_dim(scores[:, 1, :], own_start, block_rows, 0)
    positive = jnp.diagonal(own_scores)
    clip_loss = lax.dynamic_slice_in_dim(logsum, own_start, block_rows, 0) - positive
    weights = jnp.exp(scores - logsum[:, None, None]).astype(jnp.bfloat16)
    partial_sums = jnp.einsum(
        "rsc,sce->re", weights, caption_slots, preferred_element_type=jnp.float32
    )
    own_rows = lax.dynamic_slice_in_dim(partial_sums, own_start, block_rows, 0) - caption_slots[
        1
    ].astype(jnp.float32)
    partial_sums = lax.dynamic_update_slice_in_dim(partial_sums, own_rows, own_start, 0)
    parts = partial_sums.astype(jnp.bfloat16).reshape(members, block_rows, width)
    grad_unit = factor * reduce_blocks(parts, "grp")
    grad_pooled = inverse_rms * (
        grad_unit - unit_rows * jnp.mean(grad_unit * unit_rows, axis=-1, keepdims=True)
    )
    spread = jnp.broadcast_to(
        grad_pooled[:, None, :] / frames, (block_rows, frames, width)
    ).reshape(block_rows * frames, width)
    gelu_out, pullback = jax.vjp(jax.nn.gelu, projected)
    grad_projected = pullback(spread)[0].astype(jnp.bfloat16)
    scale_down = 1.0 / (groups * members) ** 0.5
    contract = (((0,), (0,)), ((), ()))
    weight_term = scale_down * lax.dot_general(
        tokens, grad_projected, contract, preferred_element_type=jnp.float32
    )
    shard_rows = reduce_blocks(weight_term.reshape(groups, depth // groups, width), "dp")
    columns = width // members
    by_member = jnp.swapaxes(shard_rows.reshape(depth // groups, members, columns), 0, 1)
    grad_w = reduce_blocks(by_member, "grp")
    return (clip_loss, grad_pooled, grad_w)


def solution(mesh):
    in_specs = (P(("dp", "grp"), None), P(), P(("dp", "grp"), None), P(), P(), P())
    out_specs = (P(("dp", "grp")), P(("dp", "grp"), None), P("dp", "grp"))
    return jax.shard_map(
        on_device, mesh=mesh, in_specs=in_specs, out_specs=out_specs, check_vma=False
    )
```

```python
import jax
import jax.numpy as jnp
from jax import lax
from jax.sharding import PartitionSpec as P

SCORE_SCALE = 2.0
EPSILON = 1e-06
FLOOR = -1e30


def gather_ring(part, axis):
    size = lax.axis_size(axis)
    me = lax.axis_index(axis)
    received = [part]
    for shift in range(1, size):
        pairs = [(i, (i + shift) % size) for i in range(size)]
        received.append(lax.ppermute(part, axis, pairs))
    stacked = jnp.stack(received)
    order = (me - jnp.arange(size, dtype=jnp.int32)) % size
    return jnp.take(stacked, order, axis=0)


def reduce_blocks(blocks, axis):
    swapped = lax.all_to_all(blocks, axis, 0, 0, tiled=True)
    return jnp.sum(swapped.astype(jnp.float32), axis=0)


def on_device(tokens, weight, captions, block_owner, confusable, counts):
    members = lax.axis_size("grp")
    groups = lax.axis_size("dp")
    group_index = lax.axis_index("dp")
    member_index = lax.axis_index("grp")
    block_rows = captions.shape[0]
    width = captions.shape[1]
    depth = tokens.shape[1]
    frames = tokens.shape[0] // block_rows
    factor = SCORE_SCALE / width**0.5
    every_block = lax.all_gather(captions, "dp", axis=0, tiled=False)
    projected = jnp.dot(tokens, weight, preferred_element_type=jnp.float32)
    activated = jax.nn.gelu(projected)
    pooled = jnp.mean(activated.reshape(block_rows, frames, width), axis=1)
    inverse_rms = lax.rsqrt(jnp.mean(pooled * pooled, axis=-1, keepdims=True) + EPSILON)
    unit_rows = pooled * inverse_rms
    embedded = unit_rows.astype(jnp.bfloat16)
    group_clips = gather_ring(embedded, "grp").reshape(members * block_rows, width)
    listed = jnp.concatenate([jnp.arange(groups, dtype=jnp.int32)[:, None], confusable], axis=1)
    slot_count = listed.shape[1] + 1
    sources = block_owner[listed[group_index]]
    fetched = jnp.take(every_block, sources, axis=0)
    caption_slots = jnp.concatenate([captions[None], fetched], axis=0)
    usable = jnp.arange(slot_count, dtype=jnp.int32) < 2 + counts[group_index]
    scores = factor * jnp.einsum(
        "re,sce->rsc", group_clips, caption_slots, preferred_element_type=jnp.float32
    )
    scores = jnp.where(usable[None, :, None], scores, FLOOR)
    row_top = jnp.max(scores, axis=(1, 2))
    row_total = jnp.sum(jnp.exp(scores - row_top[:, None, None]), axis=(1, 2))
    share = jnp.broadcast_to(jnp.stack([row_top, row_total])[None], (members, 2, row_top.shape[0]))
    stats = lax.all_to_all(share, "grp", 0, 0, tiled=True)
    row_top = jnp.max(stats[:, 0], axis=0)
    row_total = jnp.sum(stats[:, 1] * jnp.exp(stats[:, 0] - row_top[None]), axis=0)
    logsum = row_top + jnp.log(row_total)
    own_start = member_index * block_rows
    own_scores = lax.dynamic_slice_in_dim(scores[:, 1, :], own_start, block_rows, 0)
    positive = jnp.diagonal(own_scores)
    clip_loss = lax.dynamic_slice_in_dim(logsum, own_start, block_rows, 0) - positive
    weights = jnp.exp(scores - logsum[:, None, None]).astype(jnp.bfloat16)
    partial_sums = jnp.einsum(
        "rsc,sce->re", weights, caption_slots, preferred_element_type=jnp.float32
    )
    own_rows = lax.dynamic_slice_in_dim(partial_sums, own_start, block_rows, 0) - caption_slots[
        1
    ].astype(jnp.float32)
    partial_sums = lax.dynamic_update_slice_in_dim(partial_sums, own_rows, own_start, 0)
    parts = partial_sums.astype(jnp.bfloat16).reshape(members, block_rows, width)
    grad_unit = factor * reduce_blocks(parts, "grp")
    grad_pooled = inverse_rms * (
        grad_unit - unit_rows * jnp.mean(grad_unit * unit_rows, axis=-1, keepdims=True)
    )
    spread = jnp.broadcast_to(
        grad_pooled[:, None, :] / frames, (block_rows, frames, width)
    ).reshape(block_rows * frames, width)
    gelu_out, pullback = jax.vjp(jax.nn.gelu, projected)
    grad_projected = pullback(spread)[0].astype(jnp.bfloat16)
    scale_down = 1.0 / (groups * members) ** 0.5
    contract = (((0,), (0,)), ((), ()))
    weight_term = scale_down * lax.dot_general(
        tokens, grad_projected, contract, preferred_element_type=jnp.float32
    )
    row_blocks = weight_term.astype(jnp.bfloat16).reshape(groups, depth // groups, width)
    shard_rows = reduce_blocks(row_blocks, "dp")
    columns = width // members
    by_member = jnp.swapaxes(shard_rows.reshape(depth // groups, members, columns), 0, 1)
    grad_w = reduce_blocks(by_member, "grp")
    return (clip_loss, grad_pooled, grad_w)


def solution(mesh):
    in_specs = (P(("dp", "grp"), None), P(), P(("dp", "grp"), None), P(), P(), P())
    out_specs = (P(("dp", "grp")), P(("dp", "grp"), None), P("dp", "grp"))
    return jax.shard_map(
        on_device, mesh=mesh, in_specs=in_specs, out_specs=out_specs, check_vma=False
    )
```

```python
import jax
import jax.numpy as jnp
from jax import lax
from jax.sharding import PartitionSpec as P

SCORE_SCALE = 2.0
EPSILON = 1e-06
FLOOR = -1e30
DP = ("chip", "core")


def gather_ring(part, axis):
    size = lax.axis_size(axis)
    me = lax.axis_index(axis)
    received = [part]
    for shift in range(1, size):
        pairs = [(i, (i + shift) % size) for i in range(size)]
        received.append(lax.ppermute(part, axis, pairs))
    stacked = jnp.stack(received)
    order = (me - jnp.arange(size, dtype=jnp.int32)) % size
    return jnp.take(stacked, order, axis=0)


def reduce_blocks(blocks, axis):
    swapped = lax.all_to_all(blocks, axis, 0, 0, tiled=True)
    return jnp.sum(swapped.astype(jnp.float32), axis=0)


def on_device(tokens, weight, captions, block_owner, confusable, counts):
    members = lax.axis_size("grp")
    groups = lax.axis_size(DP)
    group_index = lax.axis_index(DP)
    member_index = lax.axis_index("grp")
    block_rows = captions.shape[0]
    width = captions.shape[1]
    depth = tokens.shape[1]
    frames = tokens.shape[0] // block_rows
    factor = SCORE_SCALE / width**0.5
    cores = lax.axis_size("core")
    core_index = lax.axis_index("core")
    same_core = lax.all_gather(captions, "chip", axis=0, tiled=False)
    projected = jnp.dot(tokens, weight, preferred_element_type=jnp.float32)
    activated = jax.nn.gelu(projected)
    pooled = jnp.mean(activated.reshape(block_rows, frames, width), axis=1)
    inverse_rms = lax.rsqrt(jnp.mean(pooled * pooled, axis=-1, keepdims=True) + EPSILON)
    unit_rows = pooled * inverse_rms
    embedded = unit_rows.astype(jnp.bfloat16)
    group_clips = gather_ring(embedded, "grp").reshape(members * block_rows, width)
    listed = jnp.concatenate([jnp.arange(groups, dtype=jnp.int32)[:, None], confusable], axis=1)
    slot_count = listed.shape[1] + 1
    sources = block_owner[listed[group_index]]
    partner_sources = block_owner[listed[group_index + 1 - 2 * core_index]]
    outgoing = jnp.take(same_core, partner_sources // cores, axis=0)
    incoming = lax.ppermute(outgoing, "core", [(i, (i + 1) % cores) for i in range(cores)])
    local = jnp.take(same_core, sources // cores, axis=0)
    mine = (sources % cores == core_index)[:, None, None]
    fetched = jnp.where(mine, local, incoming)
    caption_slots = jnp.concatenate([captions[None], fetched], axis=0)
    usable = jnp.arange(slot_count, dtype=jnp.int32) < 2 + counts[group_index]
    scores = factor * jnp.einsum(
        "re,sce->rsc", group_clips, caption_slots, preferred_element_type=jnp.float32
    )
    scores = jnp.where(usable[None, :, None], scores, FLOOR)
    row_top = jnp.max(scores, axis=(1, 2))
    row_total = jnp.sum(jnp.exp(scores - row_top[:, None, None]), axis=(1, 2))
    share = jnp.broadcast_to(jnp.stack([row_top, row_total])[None], (members, 2, row_top.shape[0]))
    stats = lax.all_to_all(share, "grp", 0, 0, tiled=True)
    row_top = jnp.max(stats[:, 0], axis=0)
    row_total = jnp.sum(stats[:, 1] * jnp.exp(stats[:, 0] - row_top[None]), axis=0)
    logsum = row_top + jnp.log(row_total)
    own_start = member_index * block_rows
    own_scores = lax.dynamic_slice_in_dim(scores[:, 1, :], own_start, block_rows, 0)
    positive = jnp.diagonal(own_scores)
    clip_loss = lax.dynamic_slice_in_dim(logsum, own_start, block_rows, 0) - positive
    weights = jnp.exp(scores - logsum[:, None, None]).astype(jnp.bfloat16)
    partial_sums = jnp.einsum(
        "rsc,sce->re", weights, caption_slots, preferred_element_type=jnp.float32
    )
    own_rows = lax.dynamic_slice_in_dim(partial_sums, own_start, block_rows, 0) - caption_slots[
        1
    ].astype(jnp.float32)
    partial_sums = lax.dynamic_update_slice_in_dim(partial_sums, own_rows, own_start, 0)
    parts = partial_sums.astype(jnp.bfloat16).reshape(members, block_rows, width)
    grad_unit = factor * reduce_blocks(parts, "grp")
    grad_pooled = inverse_rms * (
        grad_unit - unit_rows * jnp.mean(grad_unit * unit_rows, axis=-1, keepdims=True)
    )
    spread = jnp.broadcast_to(
        grad_pooled[:, None, :] / frames, (block_rows, frames, width)
    ).reshape(block_rows * frames, width)
    gelu_out, pullback = jax.vjp(jax.nn.gelu, projected)
    grad_projected = pullback(spread)[0].astype(jnp.bfloat16)
    scale_down = 1.0 / (groups * members) ** 0.5
    contract = (((0,), (0,)), ((), ()))
    weight_term = scale_down * lax.dot_general(
        tokens, grad_projected, contract, preferred_element_type=jnp.float32
    )
    row_blocks = weight_term.astype(jnp.bfloat16).reshape(groups, depth // groups, width)
    shard_rows = reduce_blocks(row_blocks, DP)
    columns = width // members
    by_member = jnp.swapaxes(shard_rows.reshape(depth // groups, members, columns), 0, 1)
    grad_w = reduce_blocks(by_member, "grp")
    return (clip_loss, grad_pooled, grad_w)


def solution(mesh):
    cores = 2
    devices = mesh.devices.reshape(mesh.shape["dp"] // cores, cores, mesh.shape["grp"])
    fine = jax.sharding.Mesh(devices, ("chip", "core", "grp"))
    in_specs = (P(DP + ("grp",), None), P(), P(DP + ("grp",), None), P(), P(), P())
    out_specs = (P(DP + ("grp",)), P(DP + ("grp",), None), P(DP, "grp"))
    return jax.shard_map(
        on_device, mesh=fine, in_specs=in_specs, out_specs=out_specs, check_vma=False
    )
```

```python
import jax
import jax.numpy as jnp
from jax import lax
from jax.sharding import PartitionSpec as P

SCORE_SCALE = 2.0
EPSILON = 1e-06
FLOOR = -1e30
DP = ("x", "z", "core")


def gather_ring(part, axis):
    size = lax.axis_size(axis)
    me = lax.axis_index(axis)
    received = [part]
    for shift in range(1, size):
        pairs = [(i, (i + shift) % size) for i in range(size)]
        received.append(lax.ppermute(part, axis, pairs))
    stacked = jnp.stack(received)
    order = (me - jnp.arange(size, dtype=jnp.int32)) % size
    return jnp.take(stacked, order, axis=0)


def reduce_blocks(blocks, axis):
    swapped = lax.all_to_all(blocks, axis, 0, 0, tiled=True)
    return jnp.sum(swapped.astype(jnp.float32), axis=0)


def on_device(tokens, weight, captions, block_owner, confusable, counts):
    members = lax.axis_size("grp")
    groups = lax.axis_size(DP)
    group_index = lax.axis_index(DP)
    member_index = lax.axis_index("grp")
    block_rows = captions.shape[0]
    width = captions.shape[1]
    depth = tokens.shape[1]
    frames = tokens.shape[0] // block_rows
    factor = SCORE_SCALE / width**0.5
    along_z = lax.all_gather(captions, "z", axis=0, tiled=False)
    along_x = lax.all_gather(along_z, "x", axis=0, tiled=False)
    every_block = lax.all_gather(along_x, "core", axis=0, tiled=False)
    every_block = every_block.reshape((-1,) + captions.shape)
    projected = jnp.dot(tokens, weight, preferred_element_type=jnp.float32)
    activated = jax.nn.gelu(projected)
    pooled = jnp.mean(activated.reshape(block_rows, frames, width), axis=1)
    inverse_rms = lax.rsqrt(jnp.mean(pooled * pooled, axis=-1, keepdims=True) + EPSILON)
    unit_rows = pooled * inverse_rms
    embedded = unit_rows.astype(jnp.bfloat16)
    group_clips = gather_ring(embedded, "grp").reshape(members * block_rows, width)
    listed = jnp.concatenate([jnp.arange(groups, dtype=jnp.int32)[:, None], confusable], axis=1)
    slot_count = listed.shape[1] + 1
    sources = block_owner[listed[group_index]]
    cores = lax.axis_size("core")
    zs = lax.axis_size("z")
    xs = lax.axis_size("x")
    place = (sources % cores) * (xs * zs) + (sources // (cores * zs)) * zs + (sources // cores) % zs
    fetched = jnp.take(every_block, place, axis=0)
    caption_slots = jnp.concatenate([captions[None], fetched], axis=0)
    usable = jnp.arange(slot_count, dtype=jnp.int32) < 2 + counts[group_index]
    scores = factor * jnp.einsum(
        "re,sce->rsc", group_clips, caption_slots, preferred_element_type=jnp.float32
    )
    scores = jnp.where(usable[None, :, None], scores, FLOOR)
    row_top = jnp.max(scores, axis=(1, 2))
    row_total = jnp.sum(jnp.exp(scores - row_top[:, None, None]), axis=(1, 2))
    share = jnp.broadcast_to(jnp.stack([row_top, row_total])[None], (members, 2, row_top.shape[0]))
    stats = lax.all_to_all(share, "grp", 0, 0, tiled=True)
    row_top = jnp.max(stats[:, 0], axis=0)
    row_total = jnp.sum(stats[:, 1] * jnp.exp(stats[:, 0] - row_top[None]), axis=0)
    logsum = row_top + jnp.log(row_total)
    own_start = member_index * block_rows
    own_scores = lax.dynamic_slice_in_dim(scores[:, 1, :], own_start, block_rows, 0)
    positive = jnp.diagonal(own_scores)
    clip_loss = lax.dynamic_slice_in_dim(logsum, own_start, block_rows, 0) - positive
    weights = jnp.exp(scores - logsum[:, None, None]).astype(jnp.bfloat16)
    partial_sums = jnp.einsum(
        "rsc,sce->re", weights, caption_slots, preferred_element_type=jnp.float32
    )
    own_rows = lax.dynamic_slice_in_dim(partial_sums, own_start, block_rows, 0) - caption_slots[
        1
    ].astype(jnp.float32)
    partial_sums = lax.dynamic_update_slice_in_dim(partial_sums, own_rows, own_start, 0)
    parts = partial_sums.astype(jnp.bfloat16).reshape(members, block_rows, width)
    grad_unit = factor * reduce_blocks(parts, "grp")
    grad_pooled = inverse_rms * (
        grad_unit - unit_rows * jnp.mean(grad_unit * unit_rows, axis=-1, keepdims=True)
    )
    spread = jnp.broadcast_to(
        grad_pooled[:, None, :] / frames, (block_rows, frames, width)
    ).reshape(block_rows * frames, width)
    gelu_out, pullback = jax.vjp(jax.nn.gelu, projected)
    grad_projected = pullback(spread)[0].astype(jnp.bfloat16)
    scale_down = 1.0 / (groups * members) ** 0.5
    contract = (((0,), (0,)), ((), ()))
    weight_term = scale_down * lax.dot_general(
        tokens, grad_projected, contract, preferred_element_type=jnp.float32
    )
    row_blocks = weight_term.astype(jnp.bfloat16).reshape(groups, depth // groups, width)
    shard_rows = reduce_blocks(row_blocks, DP)
    columns = width // members
    by_member = jnp.swapaxes(shard_rows.reshape(depth // groups, members, columns), 0, 1)
    grad_w = reduce_blocks(by_member, "grp")
    return (clip_loss, grad_pooled, grad_w)


def solution(mesh):
    cores, zs = 2, 8
    shape = (mesh.shape["dp"] // (cores * zs), zs, cores, mesh.shape["grp"])
    fine = jax.sharding.Mesh(mesh.devices.reshape(shape), DP + ("grp",))
    in_specs = (P(DP + ("grp",), None), P(), P(DP + ("grp",), None), P(), P(), P())
    out_specs = (P(DP + ("grp",)), P(DP + ("grp",), None), P(DP, "grp"))
    return jax.shard_map(
        on_device, mesh=fine, in_specs=in_specs, out_specs=out_specs, check_vma=False
    )
```

```python
import jax
import jax.numpy as jnp
from jax import lax
from jax.sharding import PartitionSpec as P

SCORE_SCALE = 2.0
EPSILON = 1e-06
FLOOR = -1e30


def gather_ring(part, axis):
    size = lax.axis_size(axis)
    me = lax.axis_index(axis)
    received = [part]
    for shift in range(1, size):
        pairs = [(i, (i + shift) % size) for i in range(size)]
        received.append(lax.ppermute(part, axis, pairs))
    stacked = jnp.stack(received)
    order = (me - jnp.arange(size, dtype=jnp.int32)) % size
    return jnp.take(stacked, order, axis=0)


def reduce_blocks(blocks, axis):
    swapped = lax.all_to_all(blocks, axis, 0, 0, tiled=True)
    return jnp.sum(swapped.astype(jnp.float32), axis=0)


def on_device(tokens, weight, captions, block_owner, confusable, counts):
    members = lax.axis_size("grp")
    groups = lax.axis_size("dp")
    group_index = lax.axis_index("dp")
    member_index = lax.axis_index("grp")
    block_rows = captions.shape[0]
    width = captions.shape[1]
    depth = tokens.shape[1]
    frames = tokens.shape[0] // block_rows
    factor = SCORE_SCALE / width**0.5
    every_block = lax.all_gather(captions, "dp", axis=0, tiled=False)
    projected = jnp.dot(tokens, weight, preferred_element_type=jnp.float32)
    activated = jax.nn.gelu(projected)
    pooled = jnp.mean(activated.reshape(block_rows, frames, width), axis=1)
    inverse_rms = lax.rsqrt(jnp.mean(pooled * pooled, axis=-1, keepdims=True) + EPSILON)
    unit_rows = pooled * inverse_rms
    embedded = unit_rows.astype(jnp.bfloat16)
    group_clips = gather_ring(embedded, "grp").reshape(members * block_rows, width)
    listed = jnp.concatenate([jnp.arange(groups, dtype=jnp.int32)[:, None], confusable], axis=1)
    slot_count = listed.shape[1] + 1
    sources = block_owner[listed[group_index]]
    fetched = jnp.take(every_block, sources, axis=0)
    caption_slots = jnp.concatenate([captions[None], fetched], axis=0)
    usable = jnp.arange(slot_count, dtype=jnp.int32) < 2 + counts[group_index]
    scores = factor * jnp.einsum(
        "re,sce->rsc", group_clips, caption_slots, preferred_element_type=jnp.float32
    )
    scores = jnp.where(usable[None, :, None], scores, FLOOR)
    row_top = jnp.max(scores, axis=(1, 2))
    row_total = jnp.sum(jnp.exp(scores - row_top[:, None, None]), axis=(1, 2))
    share = jnp.broadcast_to(jnp.stack([row_top, row_total])[None], (members, 2, row_top.shape[0]))
    stats = lax.all_to_all(share, "grp", 0, 0, tiled=True)
    row_top = jnp.max(stats[:, 0], axis=0)
    row_total = jnp.sum(stats[:, 1] * jnp.exp(stats[:, 0] - row_top[None]), axis=0)
    logsum = row_top + jnp.log(row_total)
    own_start = member_index * block_rows
    own_scores = lax.dynamic_slice_in_dim(scores[:, 1, :], own_start, block_rows, 0)
    positive = jnp.diagonal(own_scores)
    clip_loss = lax.dynamic_slice_in_dim(logsum, own_start, block_rows, 0) - positive
    weights = jnp.exp(scores - logsum[:, None, None]).astype(jnp.bfloat16)
    partial_sums = jnp.einsum(
        "rsc,sce->re", weights, caption_slots, preferred_element_type=jnp.float32
    )
    own_rows = lax.dynamic_slice_in_dim(partial_sums, own_start, block_rows, 0) - caption_slots[
        1
    ].astype(jnp.float32)
    partial_sums = lax.dynamic_update_slice_in_dim(partial_sums, own_rows, own_start, 0)
    parts = partial_sums.astype(jnp.bfloat16).reshape(members, block_rows, width)
    grad_unit = factor * reduce_blocks(parts, "grp")
    grad_pooled = inverse_rms * (
        grad_unit - unit_rows * jnp.mean(grad_unit * unit_rows, axis=-1, keepdims=True)
    )
    spread = jnp.broadcast_to(
        grad_pooled[:, None, :] / frames, (block_rows, frames, width)
    ).reshape(block_rows * frames, width)
    gelu_out, pullback = jax.vjp(jax.nn.gelu, projected)
    grad_projected = pullback(spread)[0].astype(jnp.bfloat16)
    scale_down = 1.0 / (groups * members) ** 0.5
    contract = (((0,), (0,)), ((), ()))
    weight_term = scale_down * lax.dot_general(
        tokens, grad_projected, contract, preferred_element_type=jnp.float32
    )
    rows = depth // groups
    half = width // members // 2
    quarters = weight_term.astype(jnp.bfloat16).reshape(depth, members, 2, half)
    dp_first = quarters[:, :, 0].reshape(groups, rows, members * half)
    grp_first = jnp.swapaxes(quarters[:, :, 1], 0, 1)
    dp_rows = reduce_blocks(dp_first, "dp")
    grp_columns = reduce_blocks(grp_first, "grp")
    left = reduce_blocks(jnp.swapaxes(dp_rows.reshape(rows, members, half), 0, 1), "grp")
    right = reduce_blocks(grp_columns.reshape(groups, rows, half), "dp")
    grad_w = jnp.concatenate([left, right], axis=1)
    return (clip_loss, grad_pooled, grad_w)


def solution(mesh):
    in_specs = (P(("dp", "grp"), None), P(), P(("dp", "grp"), None), P(), P(), P())
    out_specs = (P(("dp", "grp")), P(("dp", "grp"), None), P("dp", "grp"))
    return jax.shard_map(
        on_device, mesh=mesh, in_specs=in_specs, out_specs=out_specs, check_vma=False
    )
```

```python
import jax
import jax.numpy as jnp
from jax import lax
from jax.sharding import PartitionSpec as P

SCORE_SCALE = 2.0
EPSILON = 1e-06
FLOOR = -1e30


def gather_ring(part, axis):
    size = lax.axis_size(axis)
    me = lax.axis_index(axis)
    received = [part]
    for shift in range(1, size):
        pairs = [(i, (i + shift) % size) for i in range(size)]
        received.append(lax.ppermute(part, axis, pairs))
    stacked = jnp.stack(received)
    order = (me - jnp.arange(size, dtype=jnp.int32)) % size
    return jnp.take(stacked, order, axis=0)


def reduce_blocks(blocks, axis):
    swapped = lax.all_to_all(blocks, axis, 0, 0, tiled=True)
    return jnp.sum(swapped.astype(jnp.float32), axis=0)


def on_device(tokens, weight, captions, block_owner, confusable, counts):
    members = lax.axis_size("grp")
    groups = lax.axis_size("dp")
    group_index = lax.axis_index("dp")
    member_index = lax.axis_index("grp")
    block_rows = captions.shape[0]
    width = captions.shape[1]
    depth = tokens.shape[1]
    frames = tokens.shape[0] // block_rows
    factor = SCORE_SCALE / width**0.5
    every_block = lax.all_gather(captions, "dp", axis=0, tiled=False)
    projected = jnp.dot(tokens, weight, preferred_element_type=jnp.float32)
    activated = jax.nn.gelu(projected)
    pooled = jnp.mean(activated.reshape(block_rows, frames, width), axis=1)
    inverse_rms = lax.rsqrt(jnp.mean(pooled * pooled, axis=-1, keepdims=True) + EPSILON)
    unit_rows = pooled * inverse_rms
    embedded = unit_rows.astype(jnp.bfloat16)
    group_clips = gather_ring(embedded, "grp").reshape(members * block_rows, width)
    listed = jnp.concatenate([jnp.arange(groups, dtype=jnp.int32)[:, None], confusable], axis=1)
    slot_count = listed.shape[1] + 1
    sources = block_owner[listed[group_index]]
    slot_sources = jnp.concatenate([group_index[None].astype(sources.dtype), sources])
    caption_slots = jnp.take(every_block, slot_sources, axis=0)
    usable = jnp.arange(slot_count, dtype=jnp.int32) < 2 + counts[group_index]
    scores = factor * jnp.einsum(
        "re,sce->rsc", group_clips, caption_slots, preferred_element_type=jnp.float32
    )
    scores = jnp.where(usable[None, :, None], scores, FLOOR)
    row_top = jnp.max(scores, axis=(1, 2))
    raised = jnp.exp(scores - row_top[:, None, None])
    row_total = jnp.sum(raised, axis=(1, 2))
    partial_sums = jnp.einsum(
        "rsc,sce->re", raised.astype(jnp.bfloat16), caption_slots, preferred_element_type=jnp.float32
    )
    slot = (jnp.arange(members) == member_index)[:, None, None]
    placed = jnp.where(slot, jnp.stack([row_top, row_total])[None], 0.0)
    every_stat = lax.psum(placed, "grp")
    blocks = partial_sums.astype(jnp.bfloat16).reshape(members, block_rows, width)
    received = lax.all_to_all(blocks, "grp", 0, 0, tiled=True)
    own_start = member_index * block_rows
    got = lax.dynamic_slice_in_dim(every_stat, own_start, block_rows, 2)
    tops = got[:, 0]
    totals = got[:, 1]
    top = jnp.max(tops, axis=0)
    total = jnp.sum(totals * jnp.exp(tops - top[None]), axis=0)
    logsum = top + jnp.log(total)
    share = jnp.exp(tops - logsum[None])
    own_scores = lax.dynamic_slice_in_dim(scores[:, 1, :], own_start, block_rows, 0)
    positive = jnp.diagonal(own_scores)
    clip_loss = logsum - positive
    parts = received.astype(jnp.float32) * share[:, :, None]
    own_partial = lax.dynamic_slice_in_dim(partial_sums, own_start, block_rows, 0)
    own_share = lax.dynamic_index_in_dim(share, member_index, 0, keepdims=False)
    own_part = own_partial * own_share[:, None] - caption_slots[1].astype(jnp.float32)
    own_part = own_part.astype(jnp.bfloat16).astype(jnp.float32)
    mine = (jnp.arange(members) == member_index)[:, None, None]
    parts = jnp.where(mine, own_part[None], parts)
    grad_unit = factor * jnp.sum(parts, axis=0)
    grad_pooled = inverse_rms * (
        grad_unit - unit_rows * jnp.mean(grad_unit * unit_rows, axis=-1, keepdims=True)
    )
    spread = jnp.broadcast_to(
        grad_pooled[:, None, :] / frames, (block_rows, frames, width)
    ).reshape(block_rows * frames, width)
    gelu_out, pullback = jax.vjp(jax.nn.gelu, projected)
    grad_projected = pullback(spread)[0].astype(jnp.bfloat16)
    scale_down = 1.0 / (groups * members) ** 0.5
    contract = (((0,), (0,)), ((), ()))
    weight_term = scale_down * lax.dot_general(
        tokens, grad_projected, contract, preferred_element_type=jnp.float32
    )
    row_blocks = weight_term.astype(jnp.bfloat16).reshape(groups, depth // groups, width)
    shard_rows = reduce_blocks(row_blocks, "dp")
    columns = width // members
    by_member = jnp.swapaxes(shard_rows.reshape(depth // groups, members, columns), 0, 1)
    grad_w = reduce_blocks(by_member, "grp")
    return (clip_loss, grad_pooled, grad_w)


def solution(mesh):
    in_specs = (P(("dp", "grp"), None), P(), P(("dp", "grp"), None), P(), P(), P())
    out_specs = (P(("dp", "grp")), P(("dp", "grp"), None), P("dp", "grp"))
    return jax.shard_map(
        on_device, mesh=mesh, in_specs=in_specs, out_specs=out_specs, check_vma=False
    )
```
